1024 devices in a mesh: row: 16 (over z), col: 16 (over y_lo, x, core), rep: 4 (over y_hi).
Axes of the slice: x: 4, y: 8 (y_hi: 4, y_lo: 2; y = y_hi * 2 + y_lo), z: 16, core: 2. Of those that a mesh axis runs over, the one named last changes fastest.
Arguments:
- density_blocks: bfloat16 [16, 64, 128, 256], P('row', ('col', 'rep')), may hold values from -0.5 to 0.5
- density_columns: int32 [16, 64, 2], P('row', ('col', 'rep')), may hold values from 0 to 3, as said below
- square_pattern: int32 [16, 64, 2], P('row', ('col', 'rep')), may hold values from 0 to 3
- cube_pattern: int32 [16, 64, 2], P('row', ('col', 'rep')), may hold values from 0 to 3
Outputs:
- purified: float32 [16, 64, 128, 256], P('row', ('col', 'rep'))
The draws below stay inside these ranges and needn't reach their ends.
Inputs may be any that keep to these rules, and one draw needn't show every extreme that they name: `density_columns`: the 2 block columns of one block row within one tile are all different.
All inputs are finite; a program needn't handle non-finite values.
Results may differ from the reference program's by a relative error of at most 0.0029.
Values may be sent and summed in bfloat16 or wider, within the bound.
No kernel may reach another device: no remote copies, remote signals or barrier semaphores. Data moves between devices by JAX's collectives and lax.ppermute only.
A program may use at most 32 MiB of HBM per device.

```python
import jax
import jax.numpy as jnp
from jax import lax

BLOCK = 128
BR = 4
P_SIZE = 2
Q = 2
NBLK = 64
N_ROW = 16


def draw_density_columns(key, part):
    scores = jax.random.randint(key, (N_ROW, NBLK, BR), 0, 1048576, dtype=jnp.int32)
    scores = scores * BR + jnp.arange(BR, dtype=jnp.int32)
    order = jnp.argsort(scores, axis=-1)
    return order[:, :, :P_SIZE].astype(jnp.int32)


def plant(entries, rng, smallest, largest):
    longest = entries.shape.index(max(entries.shape))
    spots = []
    for shift in (0, 1):
        where = [jax.random.randint(jax.random.fold_in(rng, axis), (), 0, length) for axis, length in enumerate(entries.shape)]
        where[longest] = (where[longest] + shift) % entries.shape[longest]
        spots.append(tuple(where))
    return entries.at[spots[0]].set(smallest).at[spots[1]].set(largest)


def steps_of(stream_key, dims, split, least, largest):
    def one(position, blocks):
        heights = jax.random.uniform(jax.random.fold_in(jax.random.fold_in(stream_key, 6), position), (blocks,), jnp.float32, least / len(split), largest / len(split))
        return jnp.repeat(jnp.exp(heights), dims[position] // blocks).reshape((-1,) + (1,) * (len(dims) - position - 1))

    factor_of = one(*split[0])
    for cut in split[1:]:
        factor_of = factor_of * one(*cut)
    return factor_of


def noise(own_key, shape, spread, reach, cuts=(), kind=jnp.bfloat16):
    factor_of = steps_of(own_key, shape, cuts, -0.22, 0.18) if cuts else 1.0
    array = jax.random.normal(own_key, shape, jnp.float32) * spread * factor_of
    return jnp.minimum(jnp.maximum(array, -reach), reach).astype(kind)


def setup_inputs(seed: int = 0) -> dict:
    streams_of = jax.random.split(jax.random.key(seed), 5)
    density_blocks = noise(streams_of[0], (N_ROW, NBLK, BLOCK, P_SIZE * BLOCK), (max(BLOCK * N_ROW // (4 * BR), 2)) ** -0.5, 0.5, ((0, 16), (1, 64)))
    density_columns = draw_density_columns(jax.random.fold_in(streams_of[4], 71), 0)
    square_pattern = plant(jax.random.randint(streams_of[2], (N_ROW, NBLK, Q), 0, BR), jax.random.fold_in(streams_of[2], 1), 0, BR - 1).astype(jnp.int32)
    cube_pattern = plant(jax.random.randint(streams_of[3], (N_ROW, NBLK, Q), 0, BR), jax.random.fold_in(streams_of[3], 1), 0, BR - 1).astype(jnp.int32)
    return dict(density_blocks=density_blocks, density_columns=density_columns, square_pattern=square_pattern, cube_pattern=cube_pattern)


def densify(blocks, columns):
    tile_count, row_count, block_size, width = blocks.shape
    slot_count = width // block_size
    tile_ids = jnp.arange(tile_count, dtype=jnp.int32)[:, None, None]
    block_rows = jnp.broadcast_to(jnp.arange(row_count, dtype=jnp.int32)[None, :, None], columns.shape)
    global_cols = (tile_ids * BR + columns).astype(jnp.int32)
    pieces = blocks.astype(jnp.float32).reshape(tile_count, row_count, block_size, slot_count, block_size)
    pieces = jnp.transpose(pieces, (0, 1, 3, 2, 4))
    dense = jnp.zeros((row_count, block_size, tile_count * BR, block_size), jnp.float32)
    dense = dense.at[block_rows, :, global_cols, :].add(pieces)
    return dense.reshape(row_count * block_size, tile_count * BR * block_size)


def extract(dense, columns, block_size):
    tile_count, row_count, slot_count = columns.shape
    grid = dense.reshape(row_count, block_size, tile_count * BR, block_size)
    tile_ids = jnp.arange(tile_count, dtype=jnp.int32)[:, None, None]
    block_rows = jnp.broadcast_to(jnp.arange(row_count, dtype=jnp.int32)[None, :, None], columns.shape)
    global_cols = (tile_ids * BR + columns).astype(jnp.int32)
    pieces = grid[block_rows, :, global_cols, :]
    pieces = jnp.transpose(pieces, (0, 1, 3, 2, 4))
    return pieces.reshape(tile_count, row_count, block_size, slot_count * block_size)


def multiply(first, second):
    return jnp.dot(first, second, precision=lax.Precision.HIGHEST, preferred_element_type=jnp.float32)


def carry_over(second_power, square_pattern, cube_pattern):
    tile_count, row_count, block_size, width = second_power.shape
    slot_count = width // block_size
    matching = (square_pattern[:, :, None, :] == cube_pattern[:, :, :, None]).astype(jnp.float32)
    split_two = second_power.astype(jnp.float32).reshape(tile_count, row_count, block_size, slot_count, block_size)
    carried = jnp.einsum("jgtu,jgxuy->jgxty", matching, split_two, precision=lax.Precision.HIGHEST)
    return carried.reshape(tile_count, row_count, block_size, cube_pattern.shape[2] * block_size)


def reference(density_blocks, density_columns, square_pattern, cube_pattern):
    block_size = density_blocks.shape[2]
    dense_x = densify(density_blocks, density_columns)
    square = multiply(dense_x, dense_x)
    second_power = extract(square, square_pattern, block_size).astype(jnp.bfloat16)
    dense_two = densify(second_power, square_pattern)
    third_power = extract(multiply(dense_two, dense_x), cube_pattern, block_size)
    carried = carry_over(second_power, square_pattern, cube_pattern)
    return 3.0 * carried - 2.0 * third_power
```

```python
import jax
import jax.numpy as jnp
from jax import lax
from jax.sharding import PartitionSpec as P

BLOCK = 128
INDEX_ROWS = 16


def with_indices(blocks, indices):
    rows, width = blocks.shape
    tail = jnp.zeros((INDEX_ROWS, width), jnp.bfloat16)
    tail = tail.at[0, : indices.shape[0]].set(indices.astype(jnp.bfloat16))
    return jnp.concatenate([blocks.astype(jnp.bfloat16), tail], axis=0)


def split_indices(gathered, slot_count):
    blocks = gathered[:, :BLOCK, :]
    indices = gathered[:, BLOCK, :slot_count].astype(jnp.int32)
    return blocks, indices


def dense_row(blocks, columns, tile_width):
    tiles, rows, width = blocks.shape
    slots = width // BLOCK
    pieces = blocks.reshape(tiles, rows, slots, BLOCK).astype(jnp.float32)
    total = None
    for p in range(slots):
        hit = columns[:, p][:, None] == jnp.arange(tile_width, dtype=jnp.int32)[None, :]
        term = jnp.where(hit[:, None, :, None], pieces[:, :, p, None, :], 0.0)
        total = term if total is None else total + term
    dense = jnp.transpose(total, (1, 0, 2, 3))
    return dense.reshape(rows, tiles * tile_width * BLOCK).astype(jnp.bfloat16)


def selected_columns(blocks, columns, targets):
    rows_k, rows, width = blocks.shape
    slots = width // BLOCK
    pieces = blocks.reshape(rows_k, rows, slots, BLOCK)
    outs = []
    for q in range(targets.shape[0]):
        chosen = jnp.zeros((rows_k, rows, BLOCK), jnp.bfloat16)
        for p in range(slots):
            hit = columns[:, p] == targets[q]
            chosen = jnp.where(hit[:, None, None], pieces[:, :, p, :], chosen)
        outs.append(chosen)
    stacked = jnp.stack(outs, axis=2)
    return stacked.reshape(rows_k * rows, targets.shape[0] * BLOCK)


def on_device(density_blocks, density_columns, square_pattern, cube_pattern):
    tile_width = 4
    own_blocks = density_blocks[0, 0]
    own_columns = density_columns[0, 0]
    own_square = square_pattern[0, 0]
    own_cube = cube_pattern[0, 0]
    slot_count = own_columns.shape[0]

    payload = with_indices(own_blocks, own_columns)
    row_all = lax.all_gather(payload, "row", axis=0, tiled=False)
    col_all = lax.all_gather(payload, ("col", "rep"), axis=0, tiled=False)
    row_blocks, row_cols = split_indices(row_all, slot_count)
    col_blocks, col_cols = split_indices(col_all, slot_count)

    left = dense_row(row_blocks, row_cols, tile_width)
    right_square = selected_columns(col_blocks, col_cols, own_square)
    square = jnp.dot(left, right_square, preferred_element_type=jnp.float32)
    second_power = square.astype(jnp.bfloat16)

    second_payload = with_indices(second_power, own_square)
    second_all = lax.all_gather(second_payload, "row", axis=0, tiled=False)
    second_blocks, second_cols = split_indices(second_all, slot_count)
    left_two = dense_row(second_blocks, second_cols, tile_width)
    right_cube = selected_columns(col_blocks, col_cols, own_cube)
    third_power = jnp.dot(left_two, right_cube, preferred_element_type=jnp.float32)

    split_two = second_power.astype(jnp.float32).reshape(BLOCK, slot_count, BLOCK)
    carried = []
    for t in range(own_cube.shape[0]):
        acc = jnp.zeros((BLOCK, BLOCK), jnp.float32)
        for u in range(slot_count):
            acc = acc + jnp.where(own_square[u] == own_cube[t], split_two[:, u, :], 0.0)
        carried.append(acc)
    carried = jnp.stack(carried, axis=1).reshape(BLOCK, own_cube.shape[0] * BLOCK)
    purified = 3.0 * carried - 2.0 * third_power
    return purified[None, None]


def solution(mesh):
    return jax.shard_map(
        on_device,
        mesh=mesh,
        in_specs=(
            P("row", ("col", "rep"), None, None),
            P("row", ("col", "rep"), None),
            P("row", ("col", "rep"), None),
            P("row", ("col", "rep"), None),
        ),
        out_specs=P("row", ("col", "rep"), None, None),
        check_vma=False,
    )
```

```python
import jax
import jax.numpy as jnp
from jax import lax
from jax.sharding import PartitionSpec as P

BLOCK = 128
INDEX_ROWS = 16
AXES = ("row", "col", "rep")


def with_indices(blocks, indices):
    rows, width = blocks.shape
    tail = jnp.zeros((INDEX_ROWS, width), jnp.bfloat16)
    tail = tail.at[0, : indices.shape[0]].set(indices.astype(jnp.bfloat16))
    return jnp.concatenate([blocks.astype(jnp.bfloat16), tail], axis=0)


def index_table(gathered, start, count):
    return gathered[:, BLOCK, start : start + count].astype(jnp.int32)


def dense_tile(blocks, columns, tile_width):
    rows_r, rows, width = blocks.shape
    slots = width // BLOCK
    pieces = blocks.reshape(rows_r, rows, slots, BLOCK).astype(jnp.float32)
    lanes = jnp.arange(tile_width, dtype=jnp.int32)
    total = None
    for p in range(slots):
        hit = columns[:, p][:, None] == lanes[None, :]
        term = jnp.where(hit[:, None, :, None], pieces[:, :, p, None, :], 0.0)
        total = term if total is None else total + term
    return total.astype(jnp.bfloat16)


def pick_columns(full, targets):
    rows_r, rows, width, _ = full.shape
    outs = []
    for q in range(targets.shape[1]):
        chosen = jnp.zeros((rows_r, rows, BLOCK), jnp.float32)
        for w in range(width):
            hit = targets[:, q] == w
            chosen = jnp.where(hit[:, None, None], full[:, :, w, :], chosen)
        outs.append(chosen)
    return jnp.stack(outs, axis=2).reshape(rows_r, rows, targets.shape[1] * BLOCK)


def skew_pairs(sizes, step, slot, side):
    n_row, n_col, n_rep = sizes
    pairs = []
    for r in range(n_row):
        for c in range(n_col):
            for l in range(n_rep):
                k = (r + c + step * l + slot) % n_row
                dst = (r * n_col + c) * n_rep + l
                if side == "left":
                    src = (k * n_col + c) * n_rep + l
                else:
                    src = (r * n_col + k) * n_rep + l
                pairs.append((src, dst))
    return pairs


def on_device(sizes, density_blocks, density_columns, square_pattern, cube_pattern):
    n_row, n_col, n_rep = sizes
    step = n_row // n_rep
    tile_width = 4
    slot_count = density_columns.shape[2]
    own_square = square_pattern[0, 0]
    own_cube = cube_pattern[0, 0]

    own_indices = jnp.concatenate(
        [density_columns[0, 0], own_square, own_cube], axis=0
    )
    payload = with_indices(density_blocks[0, 0], own_indices)
    tile = lax.all_gather(payload, "rep", axis=0, tiled=False)
    rows_r = tile.shape[0]
    tile_square = index_table(tile, slot_count, slot_count)
    tile_cube = index_table(tile, 2 * slot_count, slot_count)

    lefts = [lax.ppermute(tile, AXES, skew_pairs(sizes, step, s, "left")) for s in range(step)]
    rights = [lax.ppermute(tile, AXES, skew_pairs(sizes, step, s, "right")) for s in range(step)]

    def dense_left(parts):
        dense = [dense_tile(p[:, :BLOCK, :], index_table(p, 0, slot_count), tile_width) for p in parts]
        stacked = jnp.stack(dense, axis=2)
        return stacked.reshape(rows_r * BLOCK, len(parts) * tile_width * BLOCK)

    dense_rights = [
        dense_tile(p[:, :BLOCK, :], index_table(p, 0, slot_count), tile_width) for p in rights
    ]
    right = jnp.stack(dense_rights, axis=0).reshape(
        len(rights) * rows_r * BLOCK, tile_width * BLOCK
    )

    left = dense_left(lefts)
    square_full = jnp.dot(left, right, preferred_element_type=jnp.float32)
    square_full = square_full.reshape(rows_r, BLOCK, tile_width, BLOCK)
    partial_square = pick_columns(square_full, tile_square)
    second_power = lax.psum_scatter(
        partial_square, "rep", scatter_dimension=0, tiled=True
    )[0].astype(jnp.bfloat16)

    second_payload = with_indices(second_power, own_square)
    second_tile = lax.all_gather(second_payload, "rep", axis=0, tiled=False)
    second_lefts = [
        lax.ppermute(second_tile, AXES, skew_pairs(sizes, step, s, "left")) for s in range(step)
    ]
    left_two = dense_left(second_lefts)
    cube_full = jnp.dot(left_two, right, preferred_element_type=jnp.float32)
    cube_full = cube_full.reshape(rows_r, BLOCK, tile_width, BLOCK)
    partial_cube = pick_columns(cube_full, tile_cube)
    third_power = lax.psum_scatter(partial_cube, "rep", scatter_dimension=0, tiled=True)[0]

    split_two = second_power.astype(jnp.float32).reshape(BLOCK, slot_count, BLOCK)
    carried = []
    for t in range(own_cube.shape[0]):
        acc = jnp.zeros((BLOCK, BLOCK), jnp.float32)
        for u in range(slot_count):
            acc = acc + jnp.where(own_square[u] == own_cube[t], split_two[:, u, :], 0.0)
        carried.append(acc)
    carried = jnp.stack(carried, axis=1).reshape(BLOCK, own_cube.shape[0] * BLOCK)
    purified = 3.0 * carried - 2.0 * third_power
    return purified[None, None]


def solution(mesh):
    sizes = (mesh.shape["row"], mesh.shape["col"], mesh.shape["rep"])

    def body(*args):
        return on_device(sizes, *args)

    return jax.shard_map(
        body,
        mesh=mesh,
        in_specs=(
            P("row", ("col", "rep"), None, None),
            P("row", ("col", "rep"), None),
            P("row", ("col", "rep"), None),
            P("row", ("col", "rep"), None),
        ),
        out_specs=P("row", ("col", "rep"), None, None),
        check_vma=False,
    )
```

```python
import jax
import jax.numpy as jnp
from jax import lax
from jax.sharding import PartitionSpec as P

BLOCK = 128
INDEX_ROWS = 16
AXES = ("row", "col", "rep")


def with_indices(blocks, indices):
    rows, width = blocks.shape
    tail = jnp.zeros((INDEX_ROWS, width), jnp.bfloat16)
    tail = tail.at[0, : indices.shape[0]].set(indices.astype(jnp.bfloat16))
    return jnp.concatenate([blocks.astype(jnp.bfloat16), tail], axis=0)


def index_table(gathered, start, count):
    return gathered[:, BLOCK, start : start + count].astype(jnp.int32)


def dense_tile(blocks, columns, tile_width):
    rows_r, rows, width = blocks.shape
    slots = width // BLOCK
    pieces = blocks.reshape(rows_r, rows, slots, BLOCK).astype(jnp.float32)
    lanes = jnp.arange(tile_width, dtype=jnp.int32)
    total = None
    for p in range(slots):
        hit = columns[:, p][:, None] == lanes[None, :]
        term = jnp.where(hit[:, None, :, None], pieces[:, :, p, None, :], 0.0)
        total = term if total is None else total + term
    return total.astype(jnp.bfloat16)


def pick_columns(full, targets):
    rows_r, rows, width, _ = full.shape
    outs = []
    for q in range(targets.shape[1]):
        chosen = jnp.zeros((rows_r, rows, BLOCK), jnp.float32)
        for w in range(width):
            hit = targets[:, q] == w
            chosen = jnp.where(hit[:, None, None], full[:, :, w, :], chosen)
        outs.append(chosen)
    return jnp.stack(outs, axis=2).reshape(rows_r, rows, targets.shape[1] * BLOCK)


def skew_pairs(sizes, step, slot, side):
    n_row, n_col, n_rep = sizes
    pairs = []
    for r in range(n_row):
        for c in range(n_col):
            for l in range(n_rep):
                k = (r + c + l + n_rep * slot) % n_row
                dst = (r * n_col + c) * n_rep + l
                if side == "left":
                    src = (k * n_col + c) * n_rep + l
                else:
                    src = (r * n_col + k) * n_rep + l
                pairs.append((src, dst))
    return pairs


def rep_gather(x, n_rep):
    me = lax.axis_index("rep")
    parts = [x]
    for d in range(1, n_rep):
        pairs = [((i + d) % n_rep, i) for i in range(n_rep)]
        parts.append(lax.ppermute(x, "rep", pairs))
    stacked = jnp.stack(parts + parts, axis=0)
    start = (n_rep - me) % n_rep
    return lax.dynamic_slice_in_dim(stacked, start, n_rep, axis=0)


def rep_reduce_scatter(partial, n_rep):
    me = lax.axis_index("rep")
    total = lax.dynamic_index_in_dim(partial, me, axis=0, keepdims=False)
    for d in range(1, n_rep):
        pairs = [(i, (i + d) % n_rep) for i in range(n_rep)]
        piece = lax.dynamic_index_in_dim(partial, (me + d) % n_rep, axis=0, keepdims=False)
        total = total + lax.ppermute(piece, "rep", pairs)
    return total


def on_device(sizes, density_blocks, density_columns, square_pattern, cube_pattern):
    n_row, n_col, n_rep = sizes
    step = n_row // n_rep
    tile_width = 4
    slot_count = density_columns.shape[2]
    own_square = square_pattern[0, 0]
    own_cube = cube_pattern[0, 0]

    own_indices = jnp.concatenate(
        [density_columns[0, 0], own_square, own_cube], axis=0
    )
    payload = with_indices(density_blocks[0, 0], own_indices)
    tile = rep_gather(payload, n_rep)
    rows_r = tile.shape[0]
    tile_square = index_table(tile, slot_count, slot_count)
    tile_cube = index_table(tile, 2 * slot_count, slot_count)

    lefts = [lax.ppermute(tile, AXES, skew_pairs(sizes, step, s, "left")) for s in range(step)]
    rights = [lax.ppermute(tile, AXES, skew_pairs(sizes, step, s, "right")) for s in range(step)]

    def dense_left(parts):
        dense = [dense_tile(p[:, :BLOCK, :], index_table(p, 0, slot_count), tile_width) for p in parts]
        stacked = jnp.stack(dense, axis=2)
        return stacked.reshape(rows_r * BLOCK, len(parts) * tile_width * BLOCK)

    dense_rights = [
        dense_tile(p[:, :BLOCK, :], index_table(p, 0, slot_count), tile_width) for p in rights
    ]
    right = jnp.stack(dense_rights, axis=0).reshape(
        len(rights) * rows_r * BLOCK, tile_width * BLOCK
    )

    left = dense_left(lefts)
    square_full = jnp.dot(left, right, preferred_element_type=jnp.float32)
    square_full = square_full.reshape(rows_r, BLOCK, tile_width, BLOCK)
    partial_square = pick_columns(square_full, tile_square)
    second_power = rep_reduce_scatter(partial_square, n_rep).astype(jnp.bfloat16)

    second_payload = with_indices(second_power, own_square)
    second_tile = rep_gather(second_payload, n_rep)
    second_lefts = [
        lax.ppermute(second_tile, AXES, skew_pairs(sizes, step, s, "left")) for s in range(step)
    ]
    left_two = dense_left(second_lefts)
    cube_full = jnp.dot(left_two, right, preferred_element_type=jnp.float32)
    cube_full = cube_full.reshape(rows_r, BLOCK, tile_width, BLOCK)
    partial_cube = pick_columns(cube_full, tile_cube)
    third_power = rep_reduce_scatter(partial_cube, n_rep)

    split_two = second_power.astype(jnp.float32).reshape(BLOCK, slot_count, BLOCK)
    carried = []
    for t in range(own_cube.shape[0]):
        acc = jnp.zeros((BLOCK, BLOCK), jnp.float32)
        for u in range(slot_count):
            acc = acc + jnp.where(own_square[u] == own_cube[t], split_two[:, u, :], 0.0)
        carried.append(acc)
    carried = jnp.stack(carried, axis=1).reshape(BLOCK, own_cube.shape[0] * BLOCK)
    purified = 3.0 * carried - 2.0 * third_power
    return purified[None, None]


def solution(mesh):
    sizes = (mesh.shape["row"], mesh.shape["col"], mesh.shape["rep"])

    def body(*args):
        return on_device(sizes, *args)

    return jax.shard_map(
        body,
        mesh=mesh,
        in_specs=(
            P("row", ("col", "rep"), None, None),
            P("row", ("col", "rep"), None),
            P("row", ("col", "rep"), None),
            P("row", ("col", "rep"), None),
        ),
        out_specs=P("row", ("col", "rep"), None, None),
        check_vma=False,
    )
```

```python
import jax
import jax.numpy as jnp
from jax import lax
from jax.sharding import PartitionSpec as P

BLOCK = 128
INDEX_ROWS = 16
AXES = ("row", "col", "rep")


def with_indices(blocks, indices):
    rows, width = blocks.shape
    tail = jnp.zeros((INDEX_ROWS, width), jnp.bfloat16)
    tail = tail.at[0, : indices.shape[0]].set(indices.astype(jnp.bfloat16))
    return jnp.concatenate([blocks.astype(jnp.bfloat16), tail], axis=0)


def compact_tile(gathered):
    rows_r, _, width = gathered.shape
    blocks = gathered[:, :BLOCK, :].reshape(rows_r * BLOCK, width)
    tables = gathered[:, BLOCK, :]
    pad = jnp.zeros((INDEX_ROWS - rows_r, width), jnp.bfloat16)
    return jnp.concatenate([blocks, tables, pad], axis=0)


def tile_blocks(tile, rows_r):
    width = tile.shape[1]
    return tile[: rows_r * BLOCK].reshape(rows_r, BLOCK, width // BLOCK, BLOCK)


def tile_table(tile, rows_r, start, count):
    return tile[rows_r * BLOCK : rows_r * BLOCK + rows_r, start : start + count].astype(jnp.int32)


def dense_columns(blocks, columns, tile_width, repeated):
    lanes = jnp.arange(tile_width, dtype=jnp.int32)
    slots = columns.shape[-1]
    total = None
    for p in range(slots):
        hit = (columns[..., p, None] == lanes)[..., None]
        piece = blocks[..., p, None, :]
        if repeated:
            term = jnp.where(hit, piece, jnp.zeros((), blocks.dtype))
            total = term if total is None else total + term
        else:
            total = jnp.where(hit, piece, jnp.zeros((), blocks.dtype) if total is None else total)
    return total


def pick_columns(full, targets):
    rows_r, rows, width, _ = full.shape
    lanes = jnp.arange(width, dtype=jnp.int32)
    outs = []
    for q in range(targets.shape[1]):
        hit = (targets[:, q, None] == lanes)[:, None, :, None]
        chosen = jnp.sum(jnp.where(hit, full, 0.0), axis=2)
        outs.append(chosen)
    return jnp.stack(outs, axis=2).reshape(rows_r, rows, targets.shape[1] * BLOCK)


def skew_pairs(sizes, step, slot, side):
    n_row, n_col, n_rep = sizes
    pairs = []
    for r in range(n_row):
        for c in range(n_col):
            for l in range(n_rep):
                k = (r + c + l + n_rep * slot) % n_row
                dst = (r * n_col + c) * n_rep + l
                if side == "left":
                    src = (k * n_col + c) * n_rep + l
                else:
                    src = (r * n_col + k) * n_rep + l
                pairs.append((src, dst))
    return pairs


def rep_gather(x, n_rep):
    me = lax.axis_index("rep")
    parts = [x]
    for d in range(1, n_rep):
        pairs = [((i + d) % n_rep, i) for i in range(n_rep)]
        parts.append(lax.ppermute(x, "rep", pairs))
    stacked = jnp.stack(parts + parts, axis=0)
    start = (n_rep - me) % n_rep
    return lax.dynamic_slice_in_dim(stacked, start, n_rep, axis=0)


def rep_reduce_scatter(partial, n_rep):
    me = lax.axis_index("rep")
    total = lax.dynamic_index_in_dim(partial, me, axis=0, keepdims=False)
    for d in range(1, n_rep):
        pairs = [(i, (i + d) % n_rep) for i in range(n_rep)]
        piece = lax.dynamic_index_in_dim(partial, (me + d) % n_rep, axis=0, keepdims=False)
        total = total + lax.ppermute(piece, "rep", pairs)
    return total


def on_device(sizes, density_blocks, density_columns, square_pattern, cube_pattern):
    n_row, n_col, n_rep = sizes
    step = n_row // n_rep
    tile_width = 4
    slot_count = density_columns.shape[2]
    own_square = square_pattern[0, 0]
    own_cube = cube_pattern[0, 0]

    own_indices = jnp.concatenate(
        [density_columns[0, 0], own_square, own_cube], axis=0
    )
    payload = with_indices(density_blocks[0, 0], own_indices)
    tile = compact_tile(rep_gather(payload, n_rep))
    rows_r = n_rep
    tile_square = tile_table(tile, rows_r, slot_count, slot_count)
    tile_cube = tile_table(tile, rows_r, 2 * slot_count, slot_count)

    lefts = [lax.ppermute(tile, AXES, skew_pairs(sizes, step, s, "left")) for s in range(step)]
    rights = [lax.ppermute(tile, AXES, skew_pairs(sizes, step, s, "right")) for s in range(step)]

    def dense_left(parts, repeated):
        blocks = jnp.stack([tile_blocks(p, rows_r) for p in parts], axis=2)
        columns = jnp.stack([tile_table(p, rows_r, 0, slot_count) for p in parts], axis=1)
        dense = dense_columns(blocks, columns[:, None, :, :], tile_width, repeated)
        return dense.reshape(rows_r * BLOCK, len(parts) * tile_width * BLOCK)

    right_blocks = jnp.stack([tile_blocks(p, rows_r) for p in rights], axis=0)
    right_columns = jnp.stack([tile_table(p, rows_r, 0, slot_count) for p in rights], axis=0)
    right = dense_columns(right_blocks, right_columns[:, :, None, :], tile_width, False)
    right = right.reshape(len(rights) * rows_r * BLOCK, tile_width * BLOCK)

    left = dense_left(lefts, False)
    square_full = jnp.dot(left, right, preferred_element_type=jnp.float32)
    square_full = square_full.reshape(rows_r, BLOCK, tile_width, BLOCK)
    partial_square = pick_columns(square_full, tile_square)
    second_power = rep_reduce_scatter(partial_square, n_rep).astype(jnp.bfloat16)

    second_payload = with_indices(second_power, own_square)
    second_tile = compact_tile(rep_gather(second_payload, n_rep))
    second_lefts = [
        lax.ppermute(second_tile, AXES, skew_pairs(sizes, step, s, "left")) for s in range(step)
    ]
    left_two = dense_left(second_lefts, True)
    cube_full = jnp.dot(left_two, right, preferred_element_type=jnp.float32)
    cube_full = cube_full.reshape(rows_r, BLOCK, tile_width, BLOCK)
    partial_cube = pick_columns(cube_full, tile_cube)
    third_power = rep_reduce_scatter(partial_cube, n_rep)

    split_two = second_power.astype(jnp.float32).reshape(BLOCK, slot_count, BLOCK)
    carried = []
    for t in range(own_cube.shape[0]):
        acc = jnp.zeros((BLOCK, BLOCK), jnp.float32)
        for u in range(slot_count):
            acc = acc + jnp.where(own_square[u] == own_cube[t], split_two[:, u, :], 0.0)
        carried.append(acc)
    carried = jnp.stack(carried, axis=1).reshape(BLOCK, own_cube.shape[0] * BLOCK)
    purified = 3.0 * carried - 2.0 * third_power
    return purified[None, None]


def solution(mesh):
    sizes = (mesh.shape["row"], mesh.shape["col"], mesh.shape["rep"])

    def body(*args):
        return on_device(sizes, *args)

    return jax.shard_map(
        body,
        mesh=mesh,
        in_specs=(
            P("row", ("col", "rep"), None, None),
            P("row", ("col", "rep"), None),
            P("row", ("col", "rep"), None),
            P("row", ("col", "rep"), None),
        ),
        out_specs=P("row", ("col", "rep"), None, None),
        check_vma=False,
    )
```

```python
import jax
import jax.numpy as jnp
from jax import lax
from jax.sharding import PartitionSpec as P

BLOCK = 128
INDEX_ROWS = 16
AXES = ("row", "col", "rep")


def with_indices(blocks, indices):
    rows, width = blocks.shape
    tail = jnp.zeros((INDEX_ROWS, width), jnp.bfloat16)
    tail = tail.at[0, : indices.shape[0]].set(indices.astype(jnp.bfloat16))
    return jnp.concatenate([blocks.astype(jnp.bfloat16), tail], axis=0)


def compact_tile(gathered):
    rows_r, _, width = gathered.shape
    blocks = gathered[:, :BLOCK, :].reshape(rows_r * BLOCK, width)
    tables = gathered[:, BLOCK, :]
    pad = jnp.zeros((INDEX_ROWS - rows_r, width), jnp.bfloat16)
    return jnp.concatenate([blocks, tables, pad], axis=0)


def tile_blocks(tile, rows_r):
    width = tile.shape[1]
    return tile[: rows_r * BLOCK].reshape(rows_r, BLOCK, width // BLOCK, BLOCK)


def tile_table(tile, rows_r, start, count):
    return tile[rows_r * BLOCK : rows_r * BLOCK + rows_r, start : start + count].astype(jnp.int32)


def dense_columns(blocks, columns, tile_width, repeated):
    lanes = jnp.arange(tile_width, dtype=jnp.int32)
    slots = columns.shape[-1]
    total = None
    for p in range(slots):
        hit = (columns[..., p, None] == lanes)[..., None]
        piece = blocks[..., p, None, :]
        if repeated:
            term = jnp.where(hit, piece, jnp.zeros((), blocks.dtype))
            total = term if total is None else total + term
        else:
            total = jnp.where(hit, piece, jnp.zeros((), blocks.dtype) if total is None else total)
    return total


def pick_columns(full, targets):
    rows_r, rows, width, _ = full.shape
    lanes = jnp.arange(width, dtype=jnp.int32)
    outs = []
    for q in range(targets.shape[1]):
        hit = (targets[:, q, None] == lanes)[:, None, :, None]
        chosen = jnp.sum(jnp.where(hit, full, 0.0), axis=2)
        outs.append(chosen)
    return jnp.stack(outs, axis=2).reshape(rows_r, rows, targets.shape[1] * BLOCK)


def skew_pairs(sizes, step, slot, side):
    n_row, n_col, n_rep = sizes
    pairs = []
    for r in range(n_row):
        for c in range(n_col):
            for l in range(n_rep):
                sign = 1 if c % 2 == 0 else -1
                k = (r + c + sign * l + n_rep * slot) % n_row
                dst = (r * n_col + c) * n_rep + l
                if side == "left":
                    src = (k * n_col + c) * n_rep + l
                else:
                    src = (r * n_col + k) * n_rep + l
                pairs.append((src, dst))
    return pairs


def rep_gather(x, n_rep):
    me = lax.axis_index("rep")
    parts = [x]
    for d in range(1, n_rep):
        pairs = [((i + d) % n_rep, i) for i in range(n_rep)]
        parts.append(lax.ppermute(x, "rep", pairs))
    stacked = jnp.stack(parts + parts, axis=0)
    start = (n_rep - me) % n_rep
    return lax.dynamic_slice_in_dim(stacked, start, n_rep, axis=0)


def rep_reduce_scatter(partial, n_rep):
    me = lax.axis_index("rep")
    total = lax.dynamic_index_in_dim(partial, me, axis=0, keepdims=False)
    for d in range(1, n_rep):
        pairs = [(i, (i + d) % n_rep) for i in range(n_rep)]
        piece = lax.dynamic_index_in_dim(partial, (me + d) % n_rep, axis=0, keepdims=False)
        total = total + lax.ppermute(piece, "rep", pairs)
    return total


def on_device(sizes, density_blocks, density_columns, square_pattern, cube_pattern):
    n_row, n_col, n_rep = sizes
    step = n_row // n_rep
    tile_width = 4
    slot_count = density_columns.shape[2]
    own_square = square_pattern[0, 0]
    own_cube = cube_pattern[0, 0]

    own_indices = jnp.concatenate(
        [density_columns[0, 0], own_square, own_cube], axis=0
    )
    payload = with_indices(density_blocks[0, 0], own_indices)
    tile = compact_tile(rep_gather(payload, n_rep))
    rows_r = n_rep
    tile_square = tile_table(tile, rows_r, slot_count, slot_count)
    tile_cube = tile_table(tile, rows_r, 2 * slot_count, slot_count)

    lefts = [lax.ppermute(tile, AXES, skew_pairs(sizes, step, s, "left")) for s in range(step)]
    rights = [lax.ppermute(tile, AXES, skew_pairs(sizes, step, s, "right")) for s in range(step)]

    def dense_left(parts, repeated):
        blocks = jnp.stack([tile_blocks(p, rows_r) for p in parts], axis=2)
        columns = jnp.stack([tile_table(p, rows_r, 0, slot_count) for p in parts], axis=1)
        dense = dense_columns(blocks, columns[:, None, :, :], tile_width, repeated)
        return dense.reshape(rows_r * BLOCK, len(parts) * tile_width * BLOCK)

    right_blocks = jnp.stack([tile_blocks(p, rows_r) for p in rights], axis=0)
    right_columns = jnp.stack([tile_table(p, rows_r, 0, slot_count) for p in rights], axis=0)
    right = dense_columns(right_blocks, right_columns[:, :, None, :], tile_width, False)
    right = right.reshape(len(rights) * rows_r * BLOCK, tile_width * BLOCK)

    left = dense_left(lefts, False)
    square_full = jnp.dot(left, right, preferred_element_type=jnp.float32)
    square_full = square_full.reshape(rows_r, BLOCK, tile_width, BLOCK)
    partial_square = pick_columns(square_full, tile_square)
    second_power = rep_reduce_scatter(partial_square, n_rep).astype(jnp.bfloat16)

    second_payload = with_indices(second_power, own_square)
    second_tile = compact_tile(rep_gather(second_payload, n_rep))
    second_lefts = [
        lax.ppermute(second_tile, AXES, skew_pairs(sizes, step, s, "left")) for s in range(step)
    ]
    left_two = dense_left(second_lefts, True)
    cube_full = jnp.dot(left_two, right, preferred_element_type=jnp.float32)
    cube_full = cube_full.reshape(rows_r, BLOCK, tile_width, BLOCK)
    partial_cube = pick_columns(cube_full, tile_cube)
    third_power = rep_reduce_scatter(partial_cube, n_rep)

    split_two = second_power.astype(jnp.float32).reshape(BLOCK, slot_count, BLOCK)
    carried = []
    for t in range(own_cube.shape[0]):
        acc = jnp.zeros((BLOCK, BLOCK), jnp.float32)
        for u in range(slot_count):
            acc = acc + jnp.where(own_square[u] == own_cube[t], split_two[:, u, :], 0.0)
        carried.append(acc)
    carried = jnp.stack(carried, axis=1).reshape(BLOCK, own_cube.shape[0] * BLOCK)
    purified = 3.0 * carried - 2.0 * third_power
    return purified[None, None]


def solution(mesh):
    sizes = (mesh.shape["row"], mesh.shape["col"], mesh.shape["rep"])

    def body(*args):
        return on_device(sizes, *args)

    return jax.shard_map(
        body,
        mesh=mesh,
        in_specs=(
            P("row", ("col", "rep"), None, None),
            P("row", ("col", "rep"), None),
            P("row", ("col", "rep"), None),
            P("row", ("col", "rep"), None),
        ),
        out_specs=P("row", ("col", "rep"), None, None),
        check_vma=False,
    )
```

```python
import jax
import jax.numpy as jnp
from jax import lax
from jax.sharding import PartitionSpec as P

BLOCK = 128
INDEX_ROWS = 16
AXES = ("row", "col", "rep")


def with_indices(blocks, indices):
    rows, width = blocks.shape
    tail = jnp.zeros((INDEX_ROWS, width), jnp.bfloat16)
    tail = tail.at[0, : indices.shape[0]].set(indices.astype(jnp.bfloat16))
    return jnp.concatenate([blocks.astype(jnp.bfloat16), tail], axis=0)


def compact_tile(gathered):
    rows_r, _, width = gathered.shape
    blocks = gathered[:, :BLOCK, :].reshape(rows_r * BLOCK, width)
    tables = gathered[:, BLOCK, :]
    pad = jnp.zeros((INDEX_ROWS - rows_r, width), jnp.bfloat16)
    return jnp.concatenate([blocks, tables, pad], axis=0)


def tile_blocks(tile, rows_r):
    width = tile.shape[1]
    return tile[: rows_r * BLOCK].reshape(rows_r, BLOCK, width // BLOCK, BLOCK)


def tile_table(tile, rows_r, start, count):
    return tile[rows_r * BLOCK : rows_r * BLOCK + rows_r, start : start + count].astype(jnp.int32)


def dense_columns(blocks, columns, tile_width, repeated):
    lanes = jnp.arange(tile_width, dtype=jnp.int32)
    slots = columns.shape[-1]
    total = None
    for p in range(slots):
        hit = (columns[..., p, None] == lanes)[..., None]
        piece = blocks[..., p, None, :]
        if repeated:
            term = jnp.where(hit, piece, jnp.zeros((), blocks.dtype))
            total = term if total is None else total + term
        else:
            total = jnp.where(hit, piece, jnp.zeros((), blocks.dtype) if total is None else total)
    return total


def pick_columns(full, targets):
    rows_r, rows, width, _ = full.shape
    lanes = jnp.arange(width, dtype=jnp.int32)
    outs = []
    for q in range(targets.shape[1]):
        hit = (targets[:, q, None] == lanes)[:, None, :, None]
        chosen = jnp.sum(jnp.where(hit, full, 0.0), axis=2)
        outs.append(chosen)
    return jnp.stack(outs, axis=2).reshape(rows_r, rows, targets.shape[1] * BLOCK)


def skew_pairs(sizes, step, slot, side):
    n_row, n_col, n_rep = sizes
    pairs = []
    for r in range(n_row):
        for c in range(n_col):
            for l in range(n_rep):
                sign = 1 if c % 2 == 0 else -1
                k = (r + c + sign * l + n_rep * slot) % n_row
                dst = (r * n_col + c) * n_rep + l
                if side == "left":
                    src = (k * n_col + c) * n_rep + l
                else:
                    src = (r * n_col + k) * n_rep + l
                pairs.append((src, dst))
    return pairs


def rep_gather(x, n_rep):
    me = lax.axis_index("rep")
    parts = [x]
    for d in range(1, n_rep):
        pairs = [((i + d) % n_rep, i) for i in range(n_rep)]
        parts.append(lax.ppermute(x, "rep", pairs))
    stacked = jnp.stack(parts + parts, axis=0)
    start = (n_rep - me) % n_rep
    return lax.dynamic_slice_in_dim(stacked, start, n_rep, axis=0)


def rep_reduce_scatter(partial, n_rep):
    me = lax.axis_index("rep")
    total = lax.dynamic_index_in_dim(partial, me, axis=0, keepdims=False)
    for d in range(1, n_rep):
        pairs = [(i, (i + d) % n_rep) for i in range(n_rep)]
        piece = lax.dynamic_index_in_dim(partial, (me + d) % n_rep, axis=0, keepdims=False)
        total = total + lax.ppermute(piece, "rep", pairs)
    return total


def on_device(sizes, density_blocks, density_columns, square_pattern, cube_pattern):
    n_row, n_col, n_rep = sizes
    step = n_row // n_rep
    tile_width = 4
    slot_count = density_columns.shape[2]
    own_square = square_pattern[0, 0]
    own_cube = cube_pattern[0, 0]

    own_indices = jnp.concatenate(
        [density_columns[0, 0], own_square, own_cube], axis=0
    )
    payload = with_indices(density_blocks[0, 0], own_indices)
    tile = compact_tile(rep_gather(payload, n_rep))
    rows_r = n_rep
    tile_square = tile_table(tile, rows_r, slot_count, slot_count)
    tile_cube = tile_table(tile, rows_r, 2 * slot_count, slot_count)

    row_groups = [[j + n_rep * i for i in range(step)] for j in range(n_rep)]
    col_groups = [[j + n_rep * i for i in range(n_col // n_rep)] for j in range(n_rep)]

    def class_gather(part, axis, groups):
        gathered = lax.all_gather(part, axis, axis_index_groups=groups, axis=0, tiled=False)
        return [gathered[i] for i in range(gathered.shape[0])]

    lefts = class_gather(
        lax.ppermute(tile, AXES, skew_pairs(sizes, step, 0, "left")), "row", row_groups
    )
    rights = class_gather(
        lax.ppermute(tile, AXES, skew_pairs(sizes, step, 0, "right")), "col", col_groups
    )
    turn = (lax.axis_index("col") // n_rep - lax.axis_index("row") // n_rep) % step
    doubled = jnp.stack(rights + rights, axis=0)
    rights = list(lax.dynamic_slice_in_dim(doubled, turn, step, axis=0))

    def dense_left(parts, repeated):
        blocks = jnp.stack([tile_blocks(p, rows_r) for p in parts], axis=2)
        columns = jnp.stack([tile_table(p, rows_r, 0, slot_count) for p in parts], axis=1)
        dense = dense_columns(blocks, columns[:, None, :, :], tile_width, repeated)
        return dense.reshape(rows_r * BLOCK, len(parts) * tile_width * BLOCK)

    right_blocks = jnp.stack([tile_blocks(p, rows_r) for p in rights], axis=0)
    right_columns = jnp.stack([tile_table(p, rows_r, 0, slot_count) for p in rights], axis=0)
    right = dense_columns(right_blocks, right_columns[:, :, None, :], tile_width, False)
    right = right.reshape(len(rights) * rows_r * BLOCK, tile_width * BLOCK)

    left = dense_left(lefts, False)
    square_full = jnp.dot(left, right, preferred_element_type=jnp.float32)
    square_full = square_full.reshape(rows_r, BLOCK, tile_width, BLOCK)
    partial_square = pick_columns(square_full, tile_square)
    second_power = rep_reduce_scatter(partial_square, n_rep).astype(jnp.bfloat16)

    second_payload = with_indices(second_power, own_square)
    second_tile = compact_tile(rep_gather(second_payload, n_rep))
    second_lefts = class_gather(
        lax.ppermute(second_tile, AXES, skew_pairs(sizes, step, 0, "left")), "row", row_groups
    )
    left_two = dense_left(second_lefts, True)
    cube_full = jnp.dot(left_two, right, preferred_element_type=jnp.float32)
    cube_full = cube_full.reshape(rows_r, BLOCK, tile_width, BLOCK)
    partial_cube = pick_columns(cube_full, tile_cube)
    third_power = rep_reduce_scatter(partial_cube, n_rep)

    split_two = second_power.astype(jnp.float32).reshape(BLOCK, slot_count, BLOCK)
    carried = []
    for t in range(own_cube.shape[0]):
        acc = jnp.zeros((BLOCK, BLOCK), jnp.float32)
        for u in range(slot_count):
            acc = acc + jnp.where(own_square[u] == own_cube[t], split_two[:, u, :], 0.0)
        carried.append(acc)
    carried = jnp.stack(carried, axis=1).reshape(BLOCK, own_cube.shape[0] * BLOCK)
    purified = 3.0 * carried - 2.0 * third_power
    return purified[None, None]


def solution(mesh):
    sizes = (mesh.shape["row"], mesh.shape["col"], mesh.shape["rep"])

    def body(*args):
        return on_device(sizes, *args)

    return jax.shard_map(
        body,
        mesh=mesh,
        in_specs=(
            P("row", ("col", "rep"), None, None),
            P("row", ("col", "rep"), None),
            P("row", ("col", "rep"), None),
            P("row", ("col", "rep"), None),
        ),
        out_specs=P("row", ("col", "rep"), None, None),
        check_vma=False,
    )
```

```python
import jax
import jax.numpy as jnp
from jax import lax
from jax.sharding import PartitionSpec as P

BLOCK = 128
INDEX_ROWS = 16
AXES = ("row", "col", "rep")


def with_indices(blocks, indices):
    rows, width = blocks.shape
    tail = jnp.zeros((INDEX_ROWS, width), jnp.bfloat16)
    tail = tail.at[0, : indices.shape[0]].set(indices.astype(jnp.bfloat16))
    return jnp.concatenate([blocks.astype(jnp.bfloat16), tail], axis=0)


def compact_tile(gathered):
    rows_r, _, width = gathered.shape
    blocks = gathered[:, :BLOCK, :].reshape(rows_r * BLOCK, width)
    tables = gathered[:, BLOCK, :]
    pad = jnp.zeros((INDEX_ROWS - rows_r, width), jnp.bfloat16)
    return jnp.concatenate([blocks, tables, pad], axis=0)


def tile_blocks(tile, rows_r):
    width = tile.shape[1]
    return tile[: rows_r * BLOCK].reshape(rows_r, BLOCK, width // BLOCK, BLOCK)


def tile_table(tile, rows_r, start, count):
    return tile[rows_r * BLOCK : rows_r * BLOCK + rows_r, start : start + count].astype(jnp.int32)


def dense_columns(blocks, columns, tile_width, repeated):
    lanes = jnp.arange(tile_width, dtype=jnp.int32)
    slots = columns.shape[-1]
    total = None
    for p in range(slots):
        hit = (columns[..., p, None] == lanes)[..., None]
        piece = blocks[..., p, None, :]
        if repeated:
            term = jnp.where(hit, piece, jnp.zeros((), blocks.dtype))
            total = term if total is None else total + term
        else:
            total = jnp.where(hit, piece, jnp.zeros((), blocks.dtype) if total is None else total)
    return total


def pick_columns(full, targets):
    rows_r, rows, width, _ = full.shape
    lanes = jnp.arange(width, dtype=jnp.int32)
    outs = []
    for q in range(targets.shape[1]):
        hit = (targets[:, q, None] == lanes)[:, None, :, None]
        chosen = jnp.sum(jnp.where(hit, full, 0.0), axis=2)
        outs.append(chosen)
    return jnp.stack(outs, axis=2).reshape(rows_r, rows, targets.shape[1] * BLOCK)


def skew_pairs(sizes, step, slot, side):
    n_row, n_col, n_rep = sizes
    pairs = []
    for r in range(n_row):
        for c in range(n_col):
            for l in range(n_rep):
                sign = 1 if c % 2 == 0 else -1
                k = (r + c + sign * l + n_rep * slot) % n_row
                dst = (r * n_col + c) * n_rep + l
                if side == "left":
                    src = (k * n_col + c) * n_rep + l
                else:
                    src = (r * n_col + k) * n_rep + l
                pairs.append((src, dst))
    return pairs


def rep_gather(x, n_rep):
    copies = jnp.broadcast_to(x[None], (n_rep,) + x.shape)
    return lax.all_to_all(copies, "rep", 0, 0, tiled=True)


def rep_reduce_scatter(partial, n_rep):
    parts = lax.all_to_all(partial, "rep", 0, 0, tiled=True)
    total = parts[0]
    for i in range(1, n_rep):
        total = total + parts[i]
    return total


def on_device(sizes, density_blocks, density_columns, square_pattern, cube_pattern):
    n_row, n_col, n_rep = sizes
    step = n_row // n_rep
    tile_width = 4
    slot_count = density_columns.shape[2]
    own_square = square_pattern[0, 0]
    own_cube = cube_pattern[0, 0]

    own_indices = jnp.concatenate(
        [density_columns[0, 0], own_square, own_cube], axis=0
    )
    payload = with_indices(density_blocks[0, 0], own_indices)
    tile = compact_tile(rep_gather(payload, n_rep))
    rows_r = n_rep
    tile_square = tile_table(tile, rows_r, slot_count, slot_count)
    tile_cube = tile_table(tile, rows_r, 2 * slot_count, slot_count)

    lefts = [lax.ppermute(tile, AXES, skew_pairs(sizes, step, s, "left")) for s in range(step)]
    rights = [lax.ppermute(tile, AXES, skew_pairs(sizes, step, s, "right")) for s in range(step)]

    def dense_left(parts, repeated):
        blocks = jnp.stack([tile_blocks(p, rows_r) for p in parts], axis=2)
        columns = jnp.stack([tile_table(p, rows_r, 0, slot_count) for p in parts], axis=1)
        dense = dense_columns(blocks, columns[:, None, :, :], tile_width, repeated)
        return dense.reshape(rows_r * BLOCK, len(parts) * tile_width * BLOCK)

    right_blocks = jnp.stack([tile_blocks(p, rows_r) for p in rights], axis=0)
    right_columns = jnp.stack([tile_table(p, rows_r, 0, slot_count) for p in rights], axis=0)
    right = dense_columns(right_blocks, right_columns[:, :, None, :], tile_width, False)
    right = right.reshape(len(rights) * rows_r * BLOCK, tile_width * BLOCK)

    left = dense_left(lefts, False)
    square_full = jnp.dot(left, right, preferred_element_type=jnp.float32)
    square_full = square_full.reshape(rows_r, BLOCK, tile_width, BLOCK)
    partial_square = pick_columns(square_full, tile_square)
    second_power = rep_reduce_scatter(partial_square, n_rep).astype(jnp.bfloat16)

    second_payload = with_indices(second_power, own_square)
    second_tile = compact_tile(rep_gather(second_payload, n_rep))
    second_lefts = [
        lax.ppermute(second_tile, AXES, skew_pairs(sizes, step, s, "left")) for s in range(step)
    ]
    left_two = dense_left(second_lefts, True)
    cube_full = jnp.dot(left_two, right, preferred_element_type=jnp.float32)
    cube_full = cube_full.reshape(rows_r, BLOCK, tile_width, BLOCK)
    partial_cube = pick_columns(cube_full, tile_cube)
    third_power = rep_reduce_scatter(partial_cube, n_rep)

    split_two = second_power.astype(jnp.float32).reshape(BLOCK, slot_count, BLOCK)
    carried = []
    for t in range(own_cube.shape[0]):
        acc = jnp.zeros((BLOCK, BLOCK), jnp.float32)
        for u in range(slot_count):
            acc = acc + jnp.where(own_square[u] == own_cube[t], split_two[:, u, :], 0.0)
        carried.append(acc)
    carried = jnp.stack(carried, axis=1).reshape(BLOCK, own_cube.shape[0] * BLOCK)
    purified = 3.0 * carried - 2.0 * third_power
    return purified[None, None]


def solution(mesh):
    sizes = (mesh.shape["row"], mesh.shape["col"], mesh.shape["rep"])

    def body(*args):
        return on_device(sizes, *args)

    return jax.shard_map(
        body,
        mesh=mesh,
        in_specs=(
            P("row", ("col", "rep"), None, None),
            P("row", ("col", "rep"), None),
            P("row", ("col", "rep"), None),
            P("row", ("col", "rep"), None),
        ),
        out_specs=P("row", ("col", "rep"), None, None),
        check_vma=False,
    )
```

```python
import jax
import jax.numpy as jnp
from jax import lax
from jax.sharding import PartitionSpec as P

BLOCK = 128
INDEX_ROWS = 16
AXES = ("row", "col", "rep")


def with_indices(blocks, indices):
    rows, width = blocks.shape
    tail = jnp.zeros((INDEX_ROWS, width), jnp.bfloat16)
    tail = tail.at[0, : indices.shape[0]].set(indices.astype(jnp.bfloat16))
    return jnp.concatenate([blocks.astype(jnp.bfloat16), tail], axis=0)


def compact_tile(gathered):
    rows_r, _, width = gathered.shape
    blocks = gathered[:, :BLOCK, :].reshape(rows_r * BLOCK, width)
    tables = gathered[:, BLOCK, :]
    pad = jnp.zeros((INDEX_ROWS - rows_r, width), jnp.bfloat16)
    return jnp.concatenate([blocks, tables, pad], axis=0)


def tile_blocks(tile, rows_r):
    width = tile.shape[1]
    return tile[: rows_r * BLOCK].reshape(rows_r, BLOCK, width // BLOCK, BLOCK)


def tile_table(tile, rows_r, start, count):
    return tile[rows_r * BLOCK : rows_r * BLOCK + rows_r, start : start + count].astype(jnp.int32)


def dense_columns(blocks, columns, tile_width, repeated):
    lanes = jnp.arange(tile_width, dtype=jnp.int32)
    slots = columns.shape[-1]
    total = None
    for p in range(slots):
        hit = (columns[..., p, None] == lanes)[..., None]
        piece = blocks[..., p, None, :]
        if repeated:
            term = jnp.where(hit, piece, jnp.zeros((), blocks.dtype))
            total = term if total is None else total + term
        else:
            total = jnp.where(hit, piece, jnp.zeros((), blocks.dtype) if total is None else total)
    return total


def pick_columns(full, targets):
    rows_r, rows, width, _ = full.shape
    lanes = jnp.arange(width, dtype=jnp.int32)
    outs = []
    for q in range(targets.shape[1]):
        hit = (targets[:, q, None] == lanes)[:, None, :, None]
        chosen = jnp.sum(jnp.where(hit, full, 0.0), axis=2)
        outs.append(chosen)
    return jnp.stack(outs, axis=2).reshape(rows_r, rows, targets.shape[1] * BLOCK)


def skew_pairs(sizes, step, slot, side):
    n_row, n_col, n_rep = sizes
    pairs = []
    for r in range(n_row):
        for c in range(n_col):
            for l in range(n_rep):
                sign = 1 if c % 2 == 0 else -1
                k = (r + c + sign * l + n_rep * slot) % n_row
                dst = (r * n_col + c) * n_rep + l
                if side == "left":
                    src = (k * n_col + c) * n_rep + l
                else:
                    src = (r * n_col + k) * n_rep + l
                pairs.append((src, dst))
    return pairs


def rep_gather(x, n_rep):
    copies = jnp.broadcast_to(x[None], (n_rep,) + x.shape)
    return lax.all_to_all(copies, "rep", 0, 0, tiled=True)


def rep_reduce_scatter(partial, n_rep):
    parts = lax.all_to_all(partial, "rep", 0, 0, tiled=True)
    total = parts[0]
    for i in range(1, n_rep):
        total = total + parts[i]
    return total


def on_device(sizes, density_blocks, density_columns, square_pattern, cube_pattern):
    n_row, n_col, n_rep = sizes
    step = n_row // n_rep
    tile_width = 4
    slot_count = density_columns.shape[2]
    own_square = square_pattern[0, 0]
    own_cube = cube_pattern[0, 0]

    own_indices = jnp.concatenate(
        [density_columns[0, 0], own_square, own_cube], axis=0
    )
    payload = with_indices(density_blocks[0, 0], own_indices)
    tile = compact_tile(rep_gather(payload, n_rep))
    rows_r = n_rep
    tile_square = tile_table(tile, rows_r, slot_count, slot_count)
    tile_cube = tile_table(tile, rows_r, 2 * slot_count, slot_count)

    row_groups = [[j + n_rep * i for i in range(step)] for j in range(n_rep)]
    col_groups = [[j + n_rep * i for i in range(n_col // n_rep)] for j in range(n_rep)]

    def class_gather(part, axis, groups):
        members = len(groups[0])
        copies = jnp.broadcast_to(part[None], (members,) + part.shape)
        gathered = lax.all_to_all(copies, axis, 0, 0, axis_index_groups=groups, tiled=True)
        return [gathered[i] for i in range(members)]

    lefts = class_gather(
        lax.ppermute(tile, AXES, skew_pairs(sizes, step, 0, "left")), "row", row_groups
    )
    rights = class_gather(
        lax.ppermute(tile, AXES, skew_pairs(sizes, step, 0, "right")), "col", col_groups
    )
    turn = (lax.axis_index("col") // n_rep - lax.axis_index("row") // n_rep) % step
    doubled = jnp.stack(rights + rights, axis=0)
    rights = list(lax.dynamic_slice_in_dim(doubled, turn, step, axis=0))

    def dense_left(parts, repeated):
        blocks = jnp.stack([tile_blocks(p, rows_r) for p in parts], axis=2)
        columns = jnp.stack([tile_table(p, rows_r, 0, slot_count) for p in parts], axis=1)
        dense = dense_columns(blocks, columns[:, None, :, :], tile_width, repeated)
        return dense.reshape(rows_r * BLOCK, len(parts) * tile_width * BLOCK)

    right_blocks = jnp.stack([tile_blocks(p, rows_r) for p in rights], axis=0)
    right_columns = jnp.stack([tile_table(p, rows_r, 0, slot_count) for p in rights], axis=0)
    right = dense_columns(right_blocks, right_columns[:, :, None, :], tile_width, False)
    right = right.reshape(len(rights) * rows_r * BLOCK, tile_width * BLOCK)

    left = dense_left(lefts, False)
    square_full = jnp.dot(left, right, preferred_element_type=jnp.float32)
    square_full = square_full.reshape(rows_r, BLOCK, tile_width, BLOCK)
    partial_square = pick_columns(square_full, tile_square)
    second_power = rep_reduce_scatter(partial_square, n_rep).astype(jnp.bfloat16)

    second_payload = with_indices(second_power, own_square)
    second_tile = compact_tile(rep_gather(second_payload, n_rep))
    second_lefts = class_gather(
        lax.ppermute(second_tile, AXES, skew_pairs(sizes, step, 0, "left")), "row", row_groups
    )
    left_two = dense_left(second_lefts, True)
    cube_full = jnp.dot(left_two, right, preferred_element_type=jnp.float32)
    cube_full = cube_full.reshape(rows_r, BLOCK, tile_width, BLOCK)
    partial_cube = pick_columns(cube_full, tile_cube)
    third_power = rep_reduce_scatter(partial_cube, n_rep)

    split_two = second_power.astype(jnp.float32).reshape(BLOCK, slot_count, BLOCK)
    carried = []
    for t in range(own_cube.shape[0]):
        acc = jnp.zeros((BLOCK, BLOCK), jnp.float32)
        for u in range(slot_count):
            acc = acc + jnp.where(own_square[u] == own_cube[t], split_two[:, u, :], 0.0)
        carried.append(acc)
    carried = jnp.stack(carried, axis=1).reshape(BLOCK, own_cube.shape[0] * BLOCK)
    purified = 3.0 * carried - 2.0 * third_power
    return purified[None, None]


def solution(mesh):
    sizes = (mesh.shape["row"], mesh.shape["col"], mesh.shape["rep"])

    def body(*args):
        return on_device(sizes, *args)

    return jax.shard_map(
        body,
        mesh=mesh,
        in_specs=(
            P("row", ("col", "rep"), None, None),
            P("row", ("col", "rep"), None),
            P("row", ("col", "rep"), None),
            P("row", ("col", "rep"), None),
        ),
        out_specs=P("row", ("col", "rep"), None, None),
        check_vma=False,
    )
```

```python
import jax
import jax.numpy as jnp
from jax import lax
from jax.sharding import PartitionSpec as P

BLOCK = 128
INDEX_ROWS = 16
AXES = ("row", "col", "rep")


def with_indices(blocks, indices):
    rows, width = blocks.shape
    tail = jnp.zeros((INDEX_ROWS, width), jnp.bfloat16)
    tail = tail.at[0, : indices.shape[0]].set(indices.astype(jnp.bfloat16))
    return jnp.concatenate([blocks.astype(jnp.bfloat16), tail], axis=0)


def compact_tile(gathered):
    rows_r, _, width = gathered.shape
    blocks = gathered[:, :BLOCK, :].reshape(rows_r * BLOCK, width)
    tables = gathered[:, BLOCK, :]
    pad = jnp.zeros((INDEX_ROWS - rows_r, width), jnp.bfloat16)
    return jnp.concatenate([blocks, tables, pad], axis=0)


def tile_blocks(tile, rows_r):
    width = tile.shape[1]
    return tile[: rows_r * BLOCK].reshape(rows_r, BLOCK, width // BLOCK, BLOCK)


def tile_table(tile, rows_r, start, count):
    return tile[rows_r * BLOCK : rows_r * BLOCK + rows_r, start : start + count].astype(jnp.int32)


def dense_columns(blocks, columns, tile_width, repeated):
    lanes = jnp.arange(tile_width, dtype=jnp.int32)
    slots = columns.shape[-1]
    total = None
    for p in range(slots):
        hit = (columns[..., p, None] == lanes)[..., None]
        piece = blocks[..., p, None, :]
        if repeated:
            term = jnp.where(hit, piece, jnp.zeros((), blocks.dtype))
            total = term if total is None else total + term
        else:
            total = jnp.where(hit, piece, jnp.zeros((), blocks.dtype) if total is None else total)
    return total


def pick_columns(full, targets):
    rows_r, rows, width, _ = full.shape
    lanes = jnp.arange(width, dtype=jnp.int32)
    outs = []
    for q in range(targets.shape[1]):
        hit = (targets[:, q, None] == lanes)[:, None, :, None]
        chosen = jnp.sum(jnp.where(hit, full, 0.0), axis=2)
        outs.append(chosen)
    return jnp.stack(outs, axis=2).reshape(rows_r, rows, targets.shape[1] * BLOCK)


def skew_pairs(sizes, step, slot, side):
    n_row, n_col, n_rep = sizes
    pairs = []
    for r in range(n_row):
        for c in range(n_col):
            for l in range(n_rep):
                sign = 1 if c % 2 == 0 else -1
                k = (r + c + sign * l + n_rep * slot) % n_row
                dst = (r * n_col + c) * n_rep + l
                if side == "left":
                    src = (k * n_col + c) * n_rep + l
                else:
                    src = (r * n_col + k) * n_rep + l
                pairs.append((src, dst))
    return pairs


def rep_gather(x, n_rep):
    copies = jnp.broadcast_to(x[None], (n_rep,) + x.shape)
    return lax.all_to_all(copies, "rep", 0, 0, tiled=True)


def rep_reduce_scatter(partial, n_rep):
    parts = lax.all_to_all(partial, "rep", 0, 0, tiled=True)
    total = parts[0]
    for i in range(1, n_rep):
        total = total + parts[i]
    return total


def on_device(sizes, density_blocks, density_columns, square_pattern, cube_pattern):
    n_row, n_col, n_rep = sizes
    step = n_row // n_rep
    tile_width = 4
    slot_count = density_columns.shape[2]
    own_square = square_pattern[0, 0]
    own_cube = cube_pattern[0, 0]

    own_indices = jnp.concatenate(
        [density_columns[0, 0], own_square, own_cube], axis=0
    )
    payload = with_indices(density_blocks[0, 0], own_indices)
    tile = compact_tile(rep_gather(payload, n_rep))
    rows_r = n_rep
    tile_square = tile_table(tile, rows_r, slot_count, slot_count)
    tile_cube = tile_table(tile, rows_r, 2 * slot_count, slot_count)

    lefts = [lax.ppermute(tile, AXES, skew_pairs(sizes, step, s, "left")) for s in range(step)]
    rights = [lax.ppermute(tile, AXES, skew_pairs(sizes, step, s, "right")) for s in range(step)]

    def dense_slot(part, repeated):
        blocks = tile_blocks(part, rows_r)
        columns = tile_table(part, rows_r, 0, slot_count)
        dense = dense_columns(blocks, columns[:, None, :], tile_width, repeated)
        return dense.reshape(rows_r * BLOCK, tile_width * BLOCK)

    def slot_sum(left_parts, right_dense, repeated):
        total = None
        for part, right in zip(left_parts, right_dense):
            term = jnp.dot(dense_slot(part, repeated), right, preferred_element_type=jnp.float32)
            total = term if total is None else total + term
        return total.reshape(rows_r, BLOCK, tile_width, BLOCK)

    right_dense = [dense_slot(p, False) for p in rights]
    square_full = slot_sum(lefts, right_dense, False)
    partial_square = pick_columns(square_full, tile_square)
    second_power = rep_reduce_scatter(partial_square, n_rep).astype(jnp.bfloat16)

    second_payload = with_indices(second_power, own_square)
    second_tile = compact_tile(rep_gather(second_payload, n_rep))
    second_lefts = [
        lax.ppermute(second_tile, AXES, skew_pairs(sizes, step, s, "left")) for s in range(step)
    ]
    cube_full = slot_sum(second_lefts, right_dense, True)
    partial_cube = pick_columns(cube_full, tile_cube)
    third_power = rep_reduce_scatter(partial_cube, n_rep)

    split_two = second_power.astype(jnp.float32).reshape(BLOCK, slot_count, BLOCK)
    carried = []
    for t in range(own_cube.shape[0]):
        acc = jnp.zeros((BLOCK, BLOCK), jnp.float32)
        for u in range(slot_count):
            acc = acc + jnp.where(own_square[u] == own_cube[t], split_two[:, u, :], 0.0)
        carried.append(acc)
    carried = jnp.stack(carried, axis=1).reshape(BLOCK, own_cube.shape[0] * BLOCK)
    purified = 3.0 * carried - 2.0 * third_power
    return purified[None, None]


def solution(mesh):
    sizes = (mesh.shape["row"], mesh.shape["col"], mesh.shape["rep"])

    def body(*args):
        return on_device(sizes, *args)

    return jax.shard_map(
        body,
        mesh=mesh,
        in_specs=(
            P("row", ("col", "rep"), None, None),
            P("row", ("col", "rep"), None),
            P("row", ("col", "rep"), None),
            P("row", ("col", "rep"), None),
        ),
        out_specs=P("row", ("col", "rep"), None, None),
        check_vma=False,
    )
```

```python
import jax
import jax.numpy as jnp
from jax import lax
from jax.sharding import PartitionSpec as P

BLOCK = 128
INDEX_ROWS = 16
AXES = ("row", "col", "rep")


def with_indices(blocks, indices):
    rows, width = blocks.shape
    tail = jnp.zeros((INDEX_ROWS, width), jnp.bfloat16)
    tail = tail.at[0, : indices.shape[0]].set(indices.astype(jnp.bfloat16))
    return jnp.concatenate([blocks.astype(jnp.bfloat16), tail], axis=0)


def compact_tile(gathered):
    rows_r, _, width = gathered.shape
    blocks = gathered[:, :BLOCK, :].reshape(rows_r * BLOCK, width)
    tables = gathered[:, BLOCK, :]
    pad = jnp.zeros((INDEX_ROWS - rows_r, width), jnp.bfloat16)
    return jnp.concatenate([blocks, tables, pad], axis=0)


def tile_blocks(tile, rows_r):
    width = tile.shape[1]
    return tile[: rows_r * BLOCK].reshape(rows_r, BLOCK, width // BLOCK, BLOCK)


def tile_table(tile, rows_r, start, count):
    return tile[rows_r * BLOCK : rows_r * BLOCK + rows_r, start : start + count].astype(jnp.int32)


def dense_columns(blocks, columns, tile_width, repeated):
    lanes = jnp.arange(tile_width, dtype=jnp.int32)
    slots = columns.shape[-1]
    total = None
    for p in range(slots):
        hit = (columns[..., p, None] == lanes)[..., None]
        piece = blocks[..., p, None, :]
        if repeated:
            term = jnp.where(hit, piece, jnp.zeros((), blocks.dtype))
            total = term if total is None else total + term
        else:
            total = jnp.where(hit, piece, jnp.zeros((), blocks.dtype) if total is None else total)
    return total


def pick_columns(full, targets):
    rows_r, rows, width, _ = full.shape
    outs = []
    for q in range(targets.shape[1]):
        chosen = full[:, :, width - 1, :]
        for w in range(width - 1):
            hit = (targets[:, q] == w)[:, None, None]
            chosen = jnp.where(hit, full[:, :, w, :], chosen)
        outs.append(chosen)
    return jnp.stack(outs, axis=2).reshape(rows_r, rows, targets.shape[1] * BLOCK)


def skew_pairs(sizes, step, slot, side):
    n_row, n_col, n_rep = sizes
    pairs = []
    for r in range(n_row):
        for c in range(n_col):
            for l in range(n_rep):
                sign = 1 if c % 2 == 0 else -1
                k = (r + c + sign * l + n_rep * slot) % n_row
                dst = (r * n_col + c) * n_rep + l
                if side == "left":
                    src = (k * n_col + c) * n_rep + l
                else:
                    src = (r * n_col + k) * n_rep + l
                pairs.append((src, dst))
    return pairs


def rep_gather(x, n_rep):
    copies = jnp.broadcast_to(x[None], (n_rep,) + x.shape)
    return lax.all_to_all(copies, "rep", 0, 0, tiled=True)


def rep_reduce_scatter(partial, n_rep):
    parts = lax.all_to_all(partial, "rep", 0, 0, tiled=True)
    total = parts[0]
    for i in range(1, n_rep):
        total = total + parts[i]
    return total


def on_device(sizes, density_blocks, density_columns, square_pattern, cube_pattern):
    n_row, n_col, n_rep = sizes
    step = n_row // n_rep
    tile_width = 4
    slot_count = density_columns.shape[2]
    own_square = square_pattern[0, 0]
    own_cube = cube_pattern[0, 0]

    own_indices = jnp.concatenate(
        [density_columns[0, 0], own_square, own_cube], axis=0
    )
    payload = with_indices(density_blocks[0, 0], own_indices)
    tile = compact_tile(rep_gather(payload, n_rep))
    rows_r = n_rep
    tile_square = tile_table(tile, rows_r, slot_count, slot_count)
    tile_cube = tile_table(tile, rows_r, 2 * slot_count, slot_count)

    lefts = [lax.ppermute(tile, AXES, skew_pairs(sizes, step, s, "left")) for s in range(step)]
    rights = [lax.ppermute(tile, AXES, skew_pairs(sizes, step, s, "right")) for s in range(step)]

    def dense_left(parts, repeated):
        blocks = jnp.stack([tile_blocks(p, rows_r) for p in parts], axis=2)
        columns = jnp.stack([tile_table(p, rows_r, 0, slot_count) for p in parts], axis=1)
        dense = dense_columns(blocks, columns[:, None, :, :], tile_width, repeated)
        return dense.reshape(rows_r * BLOCK, len(parts) * tile_width * BLOCK)

    right_blocks = jnp.stack([tile_blocks(p, rows_r) for p in rights], axis=0)
    right_columns = jnp.stack([tile_table(p, rows_r, 0, slot_count) for p in rights], axis=0)
    right = dense_columns(right_blocks, right_columns[:, :, None, :], tile_width, False)
    right = right.reshape(len(rights) * rows_r * BLOCK, tile_width * BLOCK)

    left = dense_left(lefts, False)
    square_full = jnp.dot(left, right, preferred_element_type=jnp.float32)
    square_full = square_full.reshape(rows_r, BLOCK, tile_width, BLOCK)
    partial_square = pick_columns(square_full, tile_square)
    second_power = rep_reduce_scatter(partial_square, n_rep).astype(jnp.bfloat16)

    second_payload = with_indices(second_power, own_square)
    second_tile = compact_tile(rep_gather(second_payload, n_rep))
    second_lefts = [
        lax.ppermute(second_tile, AXES, skew_pairs(sizes, step, s, "left")) for s in range(step)
    ]
    left_two = dense_left(second_lefts, True)
    cube_full = jnp.dot(left_two, right, preferred_element_type=jnp.float32)
    cube_full = cube_full.reshape(rows_r, BLOCK, tile_width, BLOCK)
    partial_cube = pick_columns(cube_full, tile_cube)
    third_power = rep_reduce_scatter(partial_cube, n_rep)

    split_two = second_power.astype(jnp.float32).reshape(BLOCK, slot_count, BLOCK)
    carried = []
    for t in range(own_cube.shape[0]):
        acc = jnp.zeros((BLOCK, BLOCK), jnp.float32)
        for u in range(slot_count):
            acc = acc + jnp.where(own_square[u] == own_cube[t], split_two[:, u, :], 0.0)
        carried.append(acc)
    carried = jnp.stack(carried, axis=1).reshape(BLOCK, own_cube.shape[0] * BLOCK)
    purified = 3.0 * carried - 2.0 * third_power
    return purified[None, None]


def solution(mesh):
    sizes = (mesh.shape["row"], mesh.shape["col"], mesh.shape["rep"])

    def body(*args):
        return on_device(sizes, *args)

    return jax.shard_map(
        body,
        mesh=mesh,
        in_specs=(
            P("row", ("col", "rep"), None, None),
            P("row", ("col", "rep"), None),
            P("row", ("col", "rep"), None),
            P("row", ("col", "rep"), None),
        ),
        out_specs=P("row", ("col", "rep"), None, None),
        check_vma=False,
    )
```
